256 devices in a mesh: pair: 128 (over x, z, y), aux: 2 (over core).
Axes of the slice: x: 4, y: 4, z: 8, core: 2. Of those that a mesh axis runs over, the one named last changes fastest.
Arguments:
- amplitudes: bfloat16 [16384, 128, 128], P('pair', 'aux'), may hold values from -6 to 6
- k_term: bfloat16 [16384, 128, 128], P('pair', 'aux'), may hold values from -6 to 6
- margin_table: bfloat16 [1024, 128, 128], P('pair'), may hold values from -0.5 to 0.5
- margin_index: int32 [16384], P('pair'), may hold values from 0 to 7
- factors: bfloat16 [128, 512, 128], P('pair', 'aux'), may hold values from -6 to 6
- vir_energy: float32 [16384, 128], P('pair'), may hold values from 0.5 to 3
- occ_energy: float32 [128], replicated, may hold values from -2 to -0.3
- pair_owner: int32 [16384, 1], P('pair'), may hold values from 0 to 127; in each aligned block of 128 rows (0 to 127, 128 to 255, ...) at most 2 rows name the same one
Outputs:
- updated: bfloat16 [16384, 128, 128], P('pair', 'aux')
The draws below stay inside these ranges and needn't reach their ends.
Inputs may be any that keep to these rules, and one draw needn't show every extreme that they name: `pair_owner`: no more than 2 of the 128 pairs of one aligned block name the same owner. `margin_index`: an index into the 8 margin blocks that belong to the pair's aligned block of 128 pairs.
All inputs are finite; a program needn't handle non-finite values.
Results may differ from the reference program's by a relative error of at most 0.0055.
Values may be sent and summed in bfloat16 or wider, within the bound.
No kernel may reach another device: no remote copies, remote signals or barrier semaphores. Data moves between devices by JAX's collectives and lax.ppermute only.
A program may use at most 128 MiB of HBM per device.

```python
import math
import jax
import jax.numpy as jnp
import numpy as np
from jax import lax

NV = 128
NAUX = 512
OVL_DEV = 8
PAIR_DEV = 128
CAP = 2
NOCC = 128
NPAIRS = 16384
N_PAIR = 128


def plant(array, stream_key, low, largest):
    dims = array.shape
    index_at = [jax.random.randint(jax.random.fold_in(stream_key, axis), (), 0, dims[axis]) for axis in range(len(dims))]
    array = array.at[tuple(index_at)].set(low)
    longest = dims.index(max(dims))
    index_at[longest] = (index_at[longest] + 1) % dims[longest]
    return array.at[tuple(index_at)].set(largest)


def block_scale(own_key, dims, cuts, smallest, high):
    level = 1.0
    for axis_at, parts in cuts:
        heights = jax.random.uniform(jax.random.fold_in(jax.random.fold_in(own_key, 6), axis_at), (parts,), jnp.float32, smallest / len(cuts), high / len(cuts))
        level = level * jnp.repeat(jnp.exp(heights), dims[axis_at] // parts).reshape((-1,) + (1,) * (len(dims) - 1 - axis_at))
    return level


def deal_out(own_key, own, number, rows, count, top, most, lean):
    ranking = jax.random.permutation(own_key, count)
    crowded, common = shares(count, rows * top, most, lean, True), shares(count, rows * top, most, lean, False)
    places = jnp.arange(count)

    def named(lengths, rotation):
        used = int((lengths > 0).sum())
        fixed = max(1, used // 4)
        moved = fixed + (places - fixed + rotation * (used - fixed)) % max(1, count - fixed)
        return jnp.zeros((count,), jnp.int32).at[ranking[jnp.where(places < fixed, places, moved)]].set(jnp.asarray(lengths, jnp.int32))

    lengths = jnp.where(number % 4 == 0, named(crowded, number // 4), named(common, number - number // 4 - 1))
    mixed = jax.random.permutation(jax.random.fold_in(own, 3), count)
    giver, taker = mixed[0:count // 2 * 2:2], mixed[1:count // 2 * 2:2]
    room = jnp.minimum(lengths[giver] - 1, most - lengths[taker]) // 2
    room = jnp.where((giver == ranking[0]) | (taker == ranking[0]) | (lengths[taker] == 0), 0, jnp.maximum(room, 0))
    moved = jax.random.randint(jax.random.fold_in(own, 4), (count // 2,), 0, 1 << 20) % (room + 1)
    lengths = lengths.at[giver].add(-moved).at[taker].add(moved)
    items = jnp.searchsorted(jnp.cumsum(lengths), jnp.arange(rows * top), side="right").astype(jnp.int32)
    table = items.reshape(top, rows).T
    table = table[jax.random.permutation(jax.random.fold_in(own, 1), rows)]
    rotation = jax.random.randint(jax.random.fold_in(own, 2), (rows, 1), 0, top)
    return jnp.take_along_axis(table, (jnp.arange(top)[None, :] + rotation) % top, axis=1)


def shares(count, total, limit, lean, full):
    portions = [(1 << 20) // math.isqrt(grade ** lean) + 1 for grade in range(1, count + 1)]
    largest = limit if full else min(limit, max(-(-total // count), total * portions[0] // sum(portions)))
    least = 1 if total - largest >= count - 1 else 0
    holding, rest = [largest] + [least] * (count - 1), total - largest - least * (count - 1)
    while rest > 0:
        movable = [i for i in range(1, count) if holding[i] < largest] or [i for i in range(1, count) if holding[i] < limit]
        whole, remaining = sum([portions[i] for i in movable]), rest
        for i in movable:
            extra = min(limit - holding[i], max(1, remaining * portions[i] // whole), rest)
            holding[i] = holding[i] + extra
            rest = rest - extra
    return np.array(holding)


def bell_draw(key, dims, spread, reach, pieces=(), held_as=jnp.bfloat16):
    loudness = block_scale(key, dims, pieces, -0.22, 0.18) if pieces else 1.0
    array = jax.random.normal(key, dims, jnp.float32) * spread * loudness
    return jnp.minimum(jnp.maximum(array, -reach), reach).astype(held_as)


def setup_inputs(seed: int = 0) -> dict:
    seeds = jax.random.split(jax.random.key(seed), 9)
    amplitudes = bell_draw(seeds[0], (NPAIRS, NV, NV), 1.0, 6.0, ((0, 128), (1, 2)))
    k_term = bell_draw(seeds[1], (NPAIRS, NV, NV), 1.0, 6.0, ((0, 128), (1, 2)))
    margin_table = bell_draw(seeds[2], (N_PAIR * OVL_DEV, NV, NV), NV ** -0.5, 0.5, ((0, 128),))
    margin_index = plant(jax.random.randint(seeds[3], (NPAIRS,), 0, OVL_DEV), jax.random.fold_in(seeds[3], 1), 0, OVL_DEV - 1).astype(jnp.int32)
    factors = bell_draw(seeds[4], (NOCC, NAUX, NV), 1.0, 6.0, ((0, 128), (1, 2)))
    vir_energy = jnp.clip(0.5 + 2.5 * jax.random.uniform(seeds[5], (NPAIRS, NV), jnp.float32) ** block_scale(seeds[5], (NPAIRS, NV), ((0, 128),), -0.2, 0.2), 0.5, 3.0)
    occ_energy = jnp.clip(jax.random.uniform(seeds[6], (NOCC,), jnp.float32, -2.0, -0.3), -2.0, -0.3)
    pair_owner_keys = jax.random.split(jax.random.fold_in(seeds[7], 1), NPAIRS // PAIR_DEV)
    pair_owner_turns = jax.random.permutation(jax.random.fold_in(seeds[7], 3), NPAIRS // PAIR_DEV)
    pair_owner = jax.vmap(lambda own, number: deal_out(jax.random.fold_in(seeds[7], 2), own, number, PAIR_DEV, N_PAIR, 1, CAP, 2))(pair_owner_keys, pair_owner_turns).reshape((NPAIRS, 1))
    return dict(amplitudes=amplitudes, k_term=k_term, margin_table=margin_table, margin_index=margin_index, factors=factors, vir_energy=vir_energy, occ_energy=occ_energy, pair_owner=pair_owner)


def rounded(values):
    return lax.optimization_barrier(values.astype(jnp.bfloat16)).astype(jnp.float32)


def reference(amplitudes, k_term, margin_table, margin_index, factors, vir_energy, occ_energy, pair_owner):
    position = jnp.arange(N_PAIR * PAIR_DEV, dtype=jnp.int32)
    block_index = (position // PAIR_DEV).astype(jnp.int32)
    occ_first = block_index
    occ_second = pair_owner[:, 0].astype(jnp.int32)
    margin_row = (block_index * OVL_DEV + margin_index).astype(jnp.int32)
    cycle_scale = float(NV * NAUX * PAIR_DEV) ** -0.5

    def blocks(values):
        return values.reshape((N_PAIR, PAIR_DEV) + values.shape[1:])

    def dress(dressed, inputs):
        amp_block, rows_ovl, first, second = inputs
        margin = margin_table[rows_ovl].astype(jnp.float32)
        halfway = rounded(jnp.einsum('pca,pab->pcb', amp_block.astype(jnp.float32), margin))
        rotated = rounded(jnp.einsum('pac,pab->pcb', margin, halfway))
        factor_rows = factors[first].astype(jnp.float32)
        partial_value = rounded(jnp.einsum('pca,pqa->pcq', rotated, factor_rows))
        return dressed.at[second].add(partial_value), None

    start = jnp.zeros((N_PAIR, NV, NAUX), jnp.float32)
    dressed, _ = lax.scan(dress, start, (blocks(amplitudes), blocks(margin_row), blocks(occ_first), blocks(occ_second)))
    cycle_table = rounded(cycle_scale * jnp.einsum('jcq,jqa->jca', rounded(dressed), factors.astype(jnp.float32)))

    def update(inputs):
        amp_block, k_block, rows_ovl, first, second, energy = inputs
        margin = margin_table[rows_ovl].astype(jnp.float32)
        own_cycle = cycle_table[second]
        cycle_term = jnp.einsum('pca,pba->pcb', own_cycle, margin)
        occ_sum = occ_energy[first] + occ_energy[second]
        denominator = energy[:, :, None] + energy[:, None, :] - occ_sum[:, None, None]
        return (amp_block.astype(jnp.float32) - (cycle_term + k_block.astype(jnp.float32)) / denominator).astype(jnp.bfloat16)

    result = lax.map(update, (blocks(amplitudes), blocks(k_term), blocks(margin_row), blocks(occ_first), blocks(occ_second), blocks(vir_energy)))
    return result.reshape(amplitudes.shape)
```

```python
import jax
import jax.numpy as jnp
from jax import lax
from jax.sharding import PartitionSpec as P


def local(
    amplitudes, k_term, margin_table, margin_index, factors, vir_energy, occ_energy, pair_owner
):
    axis_pairs = lax.axis_size("pair")
    aux_count = lax.axis_size("aux")
    own_index = lax.axis_index("pair")
    aux_index = lax.axis_index("aux")
    pair_count = amplitudes.shape[0]
    row_count = amplitudes.shape[1]
    vir_width = amplitudes.shape[2]
    aux_rows = factors.shape[1]
    ovl_count = margin_table.shape[0]
    cycle_scale = float(vir_width * aux_rows * aux_count * pair_count) ** (-0.5)
    every_factor = lax.all_gather(factors[0], ("pair", "aux"), axis=0, tiled=True)
    every_factor = every_factor.reshape(axis_pairs, aux_count * aux_rows, vir_width)
    own_factors = lax.dynamic_index_in_dim(every_factor, own_index, 0, keepdims=False)
    full_amp = lax.all_gather(amplitudes, "aux", axis=1, tiled=True)
    block_pick = (margin_index[:, None] == jnp.arange(ovl_count, dtype=jnp.int32)[None, :]).astype(
        jnp.bfloat16
    )
    margin = jnp.einsum(
        "po,oab->pab", block_pick, margin_table, preferred_element_type=jnp.float32
    ).astype(jnp.bfloat16)
    halfway = jnp.einsum(
        "pca,pab->pcb", full_amp, margin, preferred_element_type=jnp.float32
    ).astype(jnp.bfloat16)
    rotated = jnp.einsum(
        "pac,pab->pcb", margin, halfway, preferred_element_type=jnp.float32
    ).astype(jnp.bfloat16)
    rotated = lax.dynamic_slice_in_dim(rotated, aux_index * row_count, row_count, 1)
    pair_dest = pair_owner[:, 0]
    owner_pick = (
        jnp.arange(axis_pairs, dtype=jnp.int32)[:, None] == pair_dest[None, :]
    ).astype(jnp.bfloat16)
    outgoing = jnp.einsum(
        "jp,pcb->jcb", owner_pick, rotated, preferred_element_type=jnp.float32
    ).astype(jnp.bfloat16)
    incoming = lax.all_to_all(outgoing, "pair", 0, 0, tiled=True)
    dressed = jnp.einsum(
        "ica,iqa->cq", incoming, every_factor, preferred_element_type=jnp.float32
    ).astype(jnp.bfloat16)
    local_cycle = jnp.dot(dressed, own_factors, preferred_element_type=jnp.float32)
    cycle_vals = (cycle_scale * local_cycle).astype(jnp.bfloat16)
    slot_back = jnp.broadcast_to(cycle_vals[None], (axis_pairs, row_count, vir_width))
    returned = lax.all_to_all(slot_back, "pair", 0, 0, tiled=True)
    own_cycle = jnp.einsum(
        "jp,jca->pca", owner_pick, returned, preferred_element_type=jnp.float32
    ).astype(jnp.bfloat16)
    cycle_term = jnp.einsum("pca,pba->pcb", own_cycle, margin, preferred_element_type=jnp.float32)
    occ_sum = occ_energy[own_index] + occ_energy[pair_dest]
    energy_rows = lax.dynamic_slice_in_dim(vir_energy, aux_index * row_count, row_count, 1)
    denominator = energy_rows[:, :, None] + vir_energy[:, None, :] - occ_sum[:, None, None]
    updated = (
        amplitudes.astype(jnp.float32) - (cycle_term + k_term.astype(jnp.float32)) / denominator
    )
    return updated.astype(jnp.bfloat16)


def solution(mesh):
    placed = (
        P("pair", "aux", None),
        P("pair", "aux", None),
        P("pair", None, None),
        P("pair"),
        P("pair", "aux", None),
        P("pair", None),
        P(),
        P("pair", None),
    )
    return jax.shard_map(
        local, mesh=mesh, in_specs=placed, out_specs=P("pair", "aux", None), check_vma=False
    )
```

```python
import jax
import jax.numpy as jnp
from jax import lax
from jax.sharding import PartitionSpec as P


def local(
    amplitudes, k_term, margin_table, margin_index, factors, vir_energy, occ_energy, pair_owner
):
    axis_pairs = lax.axis_size("pair")
    aux_count = lax.axis_size("aux")
    own_index = lax.axis_index("pair")
    aux_index = lax.axis_index("aux")
    pair_count = amplitudes.shape[0]
    row_count = amplitudes.shape[1]
    vir_width = amplitudes.shape[2]
    aux_rows = factors.shape[1]
    ovl_count = margin_table.shape[0]
    cycle_scale = float(vir_width * aux_rows * aux_count * pair_count) ** (-0.5)
    every_factor = lax.all_gather(factors[0], ("pair", "aux"), axis=0, tiled=True)
    every_factor = every_factor.reshape(axis_pairs, aux_count * aux_rows, vir_width)
    own_factors = lax.dynamic_index_in_dim(every_factor, own_index, 0, keepdims=False)
    other_amp = lax.ppermute(amplitudes, "aux", perm=[(0, 1), (1, 0)])
    full_amp = jnp.where(
        aux_index == 0,
        jnp.concatenate([amplitudes, other_amp], axis=1),
        jnp.concatenate([other_amp, amplitudes], axis=1),
    )
    block_pick = (margin_index[:, None] == jnp.arange(ovl_count, dtype=jnp.int32)[None, :]).astype(
        jnp.bfloat16
    )
    margin = jnp.einsum(
        "po,oab->pab", block_pick, margin_table, preferred_element_type=jnp.float32
    ).astype(jnp.bfloat16)
    halfway = jnp.einsum(
        "pca,pab->pcb", full_amp, margin, preferred_element_type=jnp.float32
    ).astype(jnp.bfloat16)
    rotated = jnp.einsum(
        "pac,pab->pcb", margin, halfway, preferred_element_type=jnp.float32
    ).astype(jnp.bfloat16)
    rotated = lax.dynamic_slice_in_dim(rotated, aux_index * row_count, row_count, 1)
    pair_dest = pair_owner[:, 0]
    owner_pick = (
        jnp.arange(axis_pairs, dtype=jnp.int32)[:, None] == pair_dest[None, :]
    ).astype(jnp.bfloat16)
    outgoing = jnp.einsum(
        "jp,pcb->jcb", owner_pick, rotated, preferred_element_type=jnp.float32
    ).astype(jnp.bfloat16)
    incoming = lax.all_to_all(outgoing, "pair", 0, 0, tiled=True)
    dressed = jnp.einsum(
        "ica,iqa->cq", incoming, every_factor, preferred_element_type=jnp.float32
    ).astype(jnp.bfloat16)
    local_cycle = jnp.dot(dressed, own_factors, preferred_element_type=jnp.float32)
    cycle_vals = (cycle_scale * local_cycle).astype(jnp.bfloat16)
    slot_back = jnp.broadcast_to(cycle_vals[None], (axis_pairs, row_count, vir_width))
    returned = lax.all_to_all(slot_back, "pair", 0, 0, tiled=True)
    own_cycle = jnp.einsum(
        "jp,jca->pca", owner_pick, returned, preferred_element_type=jnp.float32
    ).astype(jnp.bfloat16)
    cycle_term = jnp.einsum("pca,pba->pcb", own_cycle, margin, preferred_element_type=jnp.float32)
    occ_sum = occ_energy[own_index] + occ_energy[pair_dest]
    energy_rows = lax.dynamic_slice_in_dim(vir_energy, aux_index * row_count, row_count, 1)
    denominator = energy_rows[:, :, None] + vir_energy[:, None, :] - occ_sum[:, None, None]
    updated = (
        amplitudes.astype(jnp.float32) - (cycle_term + k_term.astype(jnp.float32)) / denominator
    )
    return updated.astype(jnp.bfloat16)


def solution(mesh):
    placed = (
        P("pair", "aux", None),
        P("pair", "aux", None),
        P("pair", None, None),
        P("pair"),
        P("pair", "aux", None),
        P("pair", None),
        P(),
        P("pair", None),
    )
    return jax.shard_map(
        local, mesh=mesh, in_specs=placed, out_specs=P("pair", "aux", None), check_vma=False
    )
```

```python
import jax
import jax.numpy as jnp
from jax import lax
from jax.sharding import PartitionSpec as P


def local(
    amplitudes, k_term, margin_table, margin_index, factors, vir_energy, occ_energy, pair_owner
):
    axis_pairs = lax.axis_size("pair")
    aux_count = lax.axis_size("aux")
    own_index = lax.axis_index("pair")
    aux_index = lax.axis_index("aux")
    pair_count = amplitudes.shape[0]
    row_count = amplitudes.shape[1]
    vir_width = amplitudes.shape[2]
    aux_rows = factors.shape[1]
    ovl_count = margin_table.shape[0]
    cycle_scale = float(vir_width * aux_rows * aux_count * pair_count) ** (-0.5)
    every_factor = lax.all_gather(factors[0], ("pair", "aux"), axis=0, tiled=True)
    every_factor = every_factor.reshape(axis_pairs, aux_count * aux_rows, vir_width)
    own_factors = lax.dynamic_index_in_dim(every_factor, own_index, 0, keepdims=False)
    other_amp = lax.ppermute(amplitudes, "aux", perm=[(0, 1), (1, 0)])
    full_amp = jnp.where(
        aux_index == 0,
        jnp.concatenate([amplitudes, other_amp], axis=1),
        jnp.concatenate([other_amp, amplitudes], axis=1),
    )
    block_pick = (margin_index[:, None] == jnp.arange(ovl_count, dtype=jnp.int32)[None, :]).astype(
        jnp.bfloat16
    )
    margin = jnp.einsum(
        "po,oab->pab", block_pick, margin_table, preferred_element_type=jnp.float32
    ).astype(jnp.bfloat16)
    halfway = jnp.einsum(
        "pca,pab->pcb", full_amp, margin, preferred_element_type=jnp.float32
    ).astype(jnp.bfloat16)
    rotated = jnp.einsum(
        "pac,pab->pcb", margin, halfway, preferred_element_type=jnp.float32
    ).astype(jnp.bfloat16)
    rotated = lax.dynamic_slice_in_dim(rotated, aux_index * row_count, row_count, 1)
    pair_dest = pair_owner[:, 0]
    owner_pick = (
        jnp.arange(axis_pairs, dtype=jnp.int32)[:, None] == pair_dest[None, :]
    ).astype(jnp.bfloat16)
    outgoing = jnp.einsum(
        "jp,pcb->jcb", owner_pick, rotated, preferred_element_type=jnp.float32
    ).astype(jnp.bfloat16)
    occ_sum = occ_energy[own_index] + occ_energy[pair_dest]
    energy_rows = lax.dynamic_slice_in_dim(vir_energy, aux_index * row_count, row_count, 1)
    denominator = energy_rows[:, :, None] + vir_energy[:, None, :] - occ_sum[:, None, None]
    inverse = 1.0 / denominator
    prior = amplitudes.astype(jnp.float32) - k_term.astype(jnp.float32) * inverse
    outgoing, prior, inverse = lax.optimization_barrier((outgoing, prior, inverse))
    incoming = lax.all_to_all(outgoing, "pair", 0, 0, tiled=True)
    dressed = jnp.einsum(
        "ica,iqa->cq", incoming, every_factor, preferred_element_type=jnp.float32
    ).astype(jnp.bfloat16)
    local_cycle = jnp.dot(dressed, own_factors, preferred_element_type=jnp.float32)
    cycle_vals = (cycle_scale * local_cycle).astype(jnp.bfloat16)
    slot_back = jnp.broadcast_to(cycle_vals[None], (axis_pairs, row_count, vir_width))
    returned = lax.all_to_all(slot_back, "pair", 0, 0, tiled=True)
    own_cycle = jnp.einsum(
        "jp,jca->pca", owner_pick, returned, preferred_element_type=jnp.float32
    ).astype(jnp.bfloat16)
    cycle_term = jnp.einsum("pca,pba->pcb", own_cycle, margin, preferred_element_type=jnp.float32)
    updated = prior - cycle_term * inverse
    return updated.astype(jnp.bfloat16)


def solution(mesh):
    placed = (
        P("pair", "aux", None),
        P("pair", "aux", None),
        P("pair", None, None),
        P("pair"),
        P("pair", "aux", None),
        P("pair", None),
        P(),
        P("pair", None),
    )
    return jax.shard_map(
        local, mesh=mesh, in_specs=placed, out_specs=P("pair", "aux", None), check_vma=False
    )
```

```python
import jax
import jax.numpy as jnp
from jax import lax
from jax.sharding import PartitionSpec as P


RING_ORDER = ((8, 4), (4, 1), (4, 32))


def ring_gather(block, size, stride, total):
    pieces = [block]
    for shift in range(1, size):
        perm = []
        for device in range(total):
            coord = (device // stride) % size
            perm.append((device, device + ((coord + shift) % size - coord) * stride))
        pieces.append(lax.ppermute(block, "pair", perm))
    return jnp.stack(pieces)


def local(
    amplitudes, k_term, margin_table, margin_index, factors, vir_energy, occ_energy, pair_owner
):
    axis_pairs = lax.axis_size("pair")
    aux_count = lax.axis_size("aux")
    own_index = lax.axis_index("pair")
    aux_index = lax.axis_index("aux")
    pair_count = amplitudes.shape[0]
    row_count = amplitudes.shape[1]
    vir_width = amplitudes.shape[2]
    aux_rows = factors.shape[1]
    ovl_count = margin_table.shape[0]
    cycle_scale = float(vir_width * aux_rows * aux_count * pair_count) ** (-0.5)
    every_factor = lax.all_gather(factors[0], ("pair", "aux"), axis=0, tiled=True)
    every_factor = every_factor.reshape(axis_pairs, aux_count * aux_rows, vir_width)
    own_factors = lax.dynamic_index_in_dim(every_factor, own_index, 0, keepdims=False)
    other_amp = lax.ppermute(amplitudes, "aux", perm=[(0, 1), (1, 0)])
    full_amp = jnp.where(
        aux_index == 0,
        jnp.concatenate([amplitudes, other_amp], axis=1),
        jnp.concatenate([other_amp, amplitudes], axis=1),
    )
    block_pick = (margin_index[:, None] == jnp.arange(ovl_count, dtype=jnp.int32)[None, :]).astype(
        jnp.bfloat16
    )
    margin = jnp.einsum(
        "po,oab->pab", block_pick, margin_table, preferred_element_type=jnp.float32
    ).astype(jnp.bfloat16)
    halfway = jnp.einsum(
        "pca,pab->pcb", full_amp, margin, preferred_element_type=jnp.float32
    ).astype(jnp.bfloat16)
    rotated = jnp.einsum(
        "pac,pab->pcb", margin, halfway, preferred_element_type=jnp.float32
    ).astype(jnp.bfloat16)
    rotated = lax.dynamic_slice_in_dim(rotated, aux_index * row_count, row_count, 1)
    pair_dest = pair_owner[:, 0]
    owner_pick = (
        jnp.arange(axis_pairs, dtype=jnp.int32)[:, None] == pair_dest[None, :]
    ).astype(jnp.bfloat16)
    outgoing = jnp.einsum(
        "jp,pcb->jcb", owner_pick, rotated, preferred_element_type=jnp.float32
    ).astype(jnp.bfloat16)
    occ_sum = occ_energy[own_index] + occ_energy[pair_dest]
    energy_rows = lax.dynamic_slice_in_dim(vir_energy, aux_index * row_count, row_count, 1)
    denominator = energy_rows[:, :, None] + vir_energy[:, None, :] - occ_sum[:, None, None]
    inverse = 1.0 / denominator
    prior = amplitudes.astype(jnp.float32) - k_term.astype(jnp.float32) * inverse
    outgoing, prior, inverse = lax.optimization_barrier((outgoing, prior, inverse))
    incoming = lax.all_to_all(outgoing, "pair", 0, 0, tiled=True)
    dressed = jnp.einsum(
        "ica,iqa->cq", incoming, every_factor, preferred_element_type=jnp.float32
    ).astype(jnp.bfloat16)
    local_cycle = jnp.dot(dressed, own_factors, preferred_element_type=jnp.float32)
    cycle_vals = (cycle_scale * local_cycle).astype(jnp.bfloat16)
    returned = cycle_vals
    ring_offset = jnp.zeros_like(pair_dest)
    ring_scale = 1
    for size, stride in RING_ORDER:
        returned = ring_gather(returned, size, stride, axis_pairs)
        own_coord = (own_index // stride) % size
        dest_coord = (pair_dest // stride) % size
        ring_offset = ring_offset + ((own_coord - dest_coord) % size) * ring_scale
        ring_scale = ring_scale * size
    returned = returned.reshape(axis_pairs, row_count, vir_width)
    offset_pick = (
        jnp.arange(axis_pairs, dtype=jnp.int32)[:, None] == ring_offset[None, :]
    ).astype(jnp.bfloat16)
    own_cycle = jnp.einsum(
        "jp,jca->pca", offset_pick, returned, preferred_element_type=jnp.float32
    ).astype(jnp.bfloat16)
    cycle_term = jnp.einsum("pca,pba->pcb", own_cycle, margin, preferred_element_type=jnp.float32)
    updated = prior - cycle_term * inverse
    return updated.astype(jnp.bfloat16)


def solution(mesh):
    placed = (
        P("pair", "aux", None),
        P("pair", "aux", None),
        P("pair", None, None),
        P("pair"),
        P("pair", "aux", None),
        P("pair", None),
        P(),
        P("pair", None),
    )
    return jax.shard_map(
        local, mesh=mesh, in_specs=placed, out_specs=P("pair", "aux", None), check_vma=False
    )
```

```python
import jax
import jax.numpy as jnp
from jax import lax
from jax.sharding import PartitionSpec as P


RING_ORDER = ((8, 4), (4, 1), (4, 32))


def ring_gather(block, size, stride, total):
    pieces = [block]
    for shift in range(1, size):
        perm = []
        for device in range(total):
            coord = (device // stride) % size
            perm.append((device, device + ((coord + shift) % size - coord) * stride))
        pieces.append(lax.ppermute(block, "pair", perm))
    return jnp.stack(pieces)


def local(
    amplitudes, k_term, margin_table, margin_index, factors, vir_energy, occ_energy, pair_owner
):
    axis_pairs = lax.axis_size("pair")
    aux_count = lax.axis_size("aux")
    own_index = lax.axis_index("pair")
    aux_index = lax.axis_index("aux")
    pair_count = amplitudes.shape[0]
    row_count = amplitudes.shape[1]
    vir_width = amplitudes.shape[2]
    aux_rows = factors.shape[1]
    ovl_count = margin_table.shape[0]
    cycle_scale = float(vir_width * aux_rows * aux_count * pair_count) ** (-0.5)
    every_factor = lax.all_gather(factors[0], "pair", axis=0, tiled=True)
    every_factor = every_factor.reshape(axis_pairs, aux_rows, vir_width)
    swap = [(0, 1), (1, 0)]
    other_amp = lax.ppermute(amplitudes, "aux", perm=swap)
    full_amp = jnp.where(
        aux_index == 0,
        jnp.concatenate([amplitudes, other_amp], axis=1),
        jnp.concatenate([other_amp, amplitudes], axis=1),
    )
    block_pick = (margin_index[:, None] == jnp.arange(ovl_count, dtype=jnp.int32)[None, :]).astype(
        jnp.bfloat16
    )
    margin = jnp.einsum(
        "po,oab->pab", block_pick, margin_table, preferred_element_type=jnp.float32
    ).astype(jnp.bfloat16)
    halfway = jnp.einsum(
        "pca,pab->pcb", full_amp, margin, preferred_element_type=jnp.float32
    ).astype(jnp.bfloat16)
    rotated = jnp.einsum(
        "pac,pab->pcb", margin, halfway, preferred_element_type=jnp.float32
    ).astype(jnp.bfloat16)
    rotated = lax.dynamic_slice_in_dim(rotated, aux_index * row_count, row_count, 1)
    pair_dest = pair_owner[:, 0]
    owner_pick = (
        jnp.arange(axis_pairs, dtype=jnp.int32)[:, None] == pair_dest[None, :]
    ).astype(jnp.bfloat16)
    outgoing = jnp.einsum(
        "jp,pcb->jcb", owner_pick, rotated, preferred_element_type=jnp.float32
    ).astype(jnp.bfloat16)
    occ_sum = occ_energy[own_index] + occ_energy[pair_dest]
    energy_rows = lax.dynamic_slice_in_dim(vir_energy, aux_index * row_count, row_count, 1)
    denominator = energy_rows[:, :, None] + vir_energy[:, None, :] - occ_sum[:, None, None]
    inverse = 1.0 / denominator
    prior = amplitudes.astype(jnp.float32) - k_term.astype(jnp.float32) * inverse
    outgoing, prior, inverse = lax.optimization_barrier((outgoing, prior, inverse))
    incoming = lax.all_to_all(outgoing, "pair", 0, 0, tiled=True)
    other_rows = lax.ppermute(incoming, "aux", perm=swap)
    all_rows = jnp.where(
        aux_index == 0,
        jnp.concatenate([incoming, other_rows], axis=1),
        jnp.concatenate([other_rows, incoming], axis=1),
    )
    dressed = jnp.einsum(
        "ica,iqa->cq", all_rows, every_factor, preferred_element_type=jnp.float32
    ).astype(jnp.bfloat16)
    half_cycle = jnp.dot(dressed, factors[0], preferred_element_type=jnp.float32)
    own_half = lax.dynamic_slice_in_dim(half_cycle, aux_index * row_count, row_count, 0)
    sent_half = lax.dynamic_slice_in_dim(half_cycle, (1 - aux_index) * row_count, row_count, 0)
    local_cycle = own_half + lax.ppermute(sent_half, "aux", perm=swap)
    cycle_vals = (cycle_scale * local_cycle).astype(jnp.bfloat16)
    returned = cycle_vals
    ring_offset = jnp.zeros_like(pair_dest)
    ring_scale = 1
    for size, stride in RING_ORDER:
        returned = ring_gather(returned, size, stride, axis_pairs)
        own_coord = (own_index // stride) % size
        dest_coord = (pair_dest // stride) % size
        ring_offset = ring_offset + ((own_coord - dest_coord) % size) * ring_scale
        ring_scale = ring_scale * size
    returned = returned.reshape(axis_pairs, row_count, vir_width)
    offset_pick = (
        jnp.arange(axis_pairs, dtype=jnp.int32)[:, None] == ring_offset[None, :]
    ).astype(jnp.bfloat16)
    own_cycle = jnp.einsum(
        "jp,jca->pca", offset_pick, returned, preferred_element_type=jnp.float32
    ).astype(jnp.bfloat16)
    cycle_term = jnp.einsum("pca,pba->pcb", own_cycle, margin, preferred_element_type=jnp.float32)
    updated = prior - cycle_term * inverse
    return updated.astype(jnp.bfloat16)


def solution(mesh):
    placed = (
        P("pair", "aux", None),
        P("pair", "aux", None),
        P("pair", None, None),
        P("pair"),
        P("pair", "aux", None),
        P("pair", None),
        P(),
        P("pair", None),
    )
    return jax.shard_map(
        local, mesh=mesh, in_specs=placed, out_specs=P("pair", "aux", None), check_vma=False
    )
```

```python
import jax
import jax.numpy as jnp
from jax import lax
from jax.sharding import PartitionSpec as P


RING_ORDER = ((8, 4), (4, 1), (4, 32))


def ring_shift(block, size, stride, total, shift):
    perm = []
    for device in range(total):
        coord = (device // stride) % size
        perm.append((device, device + ((coord + shift) % size - coord) * stride))
    return lax.ppermute(block, "pair", perm)


def ring_gather(block, size, stride, total):
    if size == 4 and block.ndim > 2 and block.shape[0] % 2 == 0:
        ahead = ring_shift(block, size, stride, total, 1)
        behind = ring_shift(block, size, stride, total, -1)
        half = block.shape[0] // 2
        across = jnp.concatenate(
            [
                ring_shift(ahead[:half], size, stride, total, 1),
                ring_shift(behind[half:], size, stride, total, -1),
            ]
        )
        return jnp.stack([block, ahead, across, behind])
    pieces = [block]
    for shift in range(1, size):
        pieces.append(ring_shift(block, size, stride, total, shift))
    return jnp.stack(pieces)


def local(
    amplitudes, k_term, margin_table, margin_index, factors, vir_energy, occ_energy, pair_owner
):
    axis_pairs = lax.axis_size("pair")
    aux_count = lax.axis_size("aux")
    own_index = lax.axis_index("pair")
    aux_index = lax.axis_index("aux")
    pair_count = amplitudes.shape[0]
    row_count = amplitudes.shape[1]
    vir_width = amplitudes.shape[2]
    aux_rows = factors.shape[1]
    ovl_count = margin_table.shape[0]
    cycle_scale = float(vir_width * aux_rows * aux_count * pair_count) ** (-0.5)
    every_factor = lax.all_gather(factors[0], ("pair", "aux"), axis=0, tiled=True)
    every_factor = every_factor.reshape(axis_pairs, aux_count * aux_rows, vir_width)
    own_factors = lax.dynamic_index_in_dim(every_factor, own_index, 0, keepdims=False)
    other_amp = lax.ppermute(amplitudes, "aux", perm=[(0, 1), (1, 0)])
    full_amp = jnp.where(
        aux_index == 0,
        jnp.concatenate([amplitudes, other_amp], axis=1),
        jnp.concatenate([other_amp, amplitudes], axis=1),
    )
    block_pick = (margin_index[:, None] == jnp.arange(ovl_count, dtype=jnp.int32)[None, :]).astype(
        jnp.bfloat16
    )
    margin = jnp.einsum(
        "po,oab->pab", block_pick, margin_table, preferred_element_type=jnp.float32
    ).astype(jnp.bfloat16)
    halfway = jnp.einsum(
        "pca,pab->pcb", full_amp, margin, preferred_element_type=jnp.float32
    ).astype(jnp.bfloat16)
    rotated = jnp.einsum(
        "pac,pab->pcb", margin, halfway, preferred_element_type=jnp.float32
    ).astype(jnp.bfloat16)
    rotated = lax.dynamic_slice_in_dim(rotated, aux_index * row_count, row_count, 1)
    pair_dest = pair_owner[:, 0]
    owner_pick = (
        jnp.arange(axis_pairs, dtype=jnp.int32)[:, None] == pair_dest[None, :]
    ).astype(jnp.bfloat16)
    outgoing = jnp.einsum(
        "jp,pcb->jcb", owner_pick, rotated, preferred_element_type=jnp.float32
    ).astype(jnp.bfloat16)
    occ_sum = occ_energy[own_index] + occ_energy[pair_dest]
    energy_rows = lax.dynamic_slice_in_dim(vir_energy, aux_index * row_count, row_count, 1)
    denominator = energy_rows[:, :, None] + vir_energy[:, None, :] - occ_sum[:, None, None]
    inverse = 1.0 / denominator
    prior = amplitudes.astype(jnp.float32) - k_term.astype(jnp.float32) * inverse
    outgoing, prior, inverse = lax.optimization_barrier((outgoing, prior, inverse))
    incoming = lax.all_to_all(outgoing, "pair", 0, 0, tiled=True)
    dressed = jnp.einsum(
        "ica,iqa->cq", incoming, every_factor, preferred_element_type=jnp.float32
    ).astype(jnp.bfloat16)
    local_cycle = jnp.dot(dressed, own_factors, preferred_element_type=jnp.float32)
    cycle_vals = (cycle_scale * local_cycle).astype(jnp.bfloat16)
    returned = cycle_vals
    ring_offset = jnp.zeros_like(pair_dest)
    ring_scale = 1
    for size, stride in RING_ORDER:
        returned = ring_gather(returned, size, stride, axis_pairs)
        own_coord = (own_index // stride) % size
        dest_coord = (pair_dest // stride) % size
        ring_offset = ring_offset + ((own_coord - dest_coord) % size) * ring_scale
        ring_scale = ring_scale * size
    returned = returned.reshape(axis_pairs, row_count, vir_width)
    offset_pick = (
        jnp.arange(axis_pairs, dtype=jnp.int32)[:, None] == ring_offset[None, :]
    ).astype(jnp.bfloat16)
    own_cycle = jnp.einsum(
        "jp,jca->pca", offset_pick, returned, preferred_element_type=jnp.float32
    ).astype(jnp.bfloat16)
    cycle_term = jnp.einsum("pca,pba->pcb", own_cycle, margin, preferred_element_type=jnp.float32)
    updated = prior - cycle_term * inverse
    return updated.astype(jnp.bfloat16)


def solution(mesh):
    placed = (
        P("pair", "aux", None),
        P("pair", "aux", None),
        P("pair", None, None),
        P("pair"),
        P("pair", "aux", None),
        P("pair", None),
        P(),
        P("pair", None),
    )
    return jax.shard_map(
        local, mesh=mesh, in_specs=placed, out_specs=P("pair", "aux", None), check_vma=False
    )
```

```python
import jax
import jax.numpy as jnp
from jax import lax
from jax.sharding import PartitionSpec as P


RING_ORDER = ((8, 4), (4, 1), (4, 32))


def ring_gather(block, size, stride, total):
    pieces = [block]
    for shift in range(1, size):
        perm = []
        for device in range(total):
            coord = (device // stride) % size
            perm.append((device, device + ((coord + shift) % size - coord) * stride))
        pieces.append(lax.ppermute(block, "pair", perm))
    return jnp.stack(pieces)


def local(
    amplitudes, k_term, margin_table, margin_index, factors, vir_energy, occ_energy, pair_owner
):
    axis_pairs = lax.axis_size("pair")
    aux_count = lax.axis_size("aux")
    own_index = lax.axis_index("pair")
    aux_index = lax.axis_index("aux")
    pair_count = amplitudes.shape[0]
    row_count = amplitudes.shape[1]
    vir_width = amplitudes.shape[2]
    aux_rows = factors.shape[1]
    ovl_count = margin_table.shape[0]
    cycle_scale = float(vir_width * aux_rows * aux_count * pair_count) ** (-0.5)
    every_factor = lax.all_gather(factors[0], "pair", axis=0, tiled=True)
    every_factor = every_factor.reshape(axis_pairs, aux_rows, vir_width)
    swap = [(0, 1), (1, 0)]
    other_amp = lax.ppermute(amplitudes, "aux", perm=swap)
    full_amp = jnp.where(
        aux_index == 0,
        jnp.concatenate([amplitudes, other_amp], axis=1),
        jnp.concatenate([other_amp, amplitudes], axis=1),
    )
    block_pick = (margin_index[:, None] == jnp.arange(ovl_count, dtype=jnp.int32)[None, :]).astype(
        jnp.bfloat16
    )
    margin = jnp.einsum(
        "po,oab->pab", block_pick, margin_table, preferred_element_type=jnp.float32
    ).astype(jnp.bfloat16)
    halfway = jnp.einsum(
        "pca,pab->pcb", full_amp, margin, preferred_element_type=jnp.float32
    ).astype(jnp.bfloat16)
    rotated = jnp.einsum(
        "pac,pab->pcb", margin, halfway, preferred_element_type=jnp.float32
    ).astype(jnp.bfloat16)
    rotated = lax.dynamic_slice_in_dim(rotated, aux_index * row_count, row_count, 1)
    pair_dest = pair_owner[:, 0]
    owner_pick = (
        jnp.arange(axis_pairs, dtype=jnp.int32)[:, None] == pair_dest[None, :]
    ).astype(jnp.bfloat16)
    outgoing = jnp.einsum(
        "jp,pcb->jcb", owner_pick, rotated, preferred_element_type=jnp.float32
    ).astype(jnp.bfloat16)
    occ_sum = occ_energy[own_index] + occ_energy[pair_dest]
    energy_rows = lax.dynamic_slice_in_dim(vir_energy, aux_index * row_count, row_count, 1)
    denominator = energy_rows[:, :, None] + vir_energy[:, None, :] - occ_sum[:, None, None]
    inverse = 1.0 / denominator
    prior = amplitudes.astype(jnp.float32) - k_term.astype(jnp.float32) * inverse
    outgoing, prior, inverse = lax.optimization_barrier((outgoing, prior, inverse))
    incoming = lax.all_to_all(outgoing, "pair", 0, 0, tiled=True)
    other_rows = lax.ppermute(incoming, "aux", perm=swap)
    all_rows = jnp.where(
        aux_index == 0,
        jnp.concatenate([incoming, other_rows], axis=1),
        jnp.concatenate([other_rows, incoming], axis=1),
    )
    dressed = jnp.einsum(
        "ica,iqa->cq", all_rows, every_factor, preferred_element_type=jnp.float32
    ).astype(jnp.bfloat16)
    half_cycle = jnp.dot(dressed, factors[0], preferred_element_type=jnp.float32)
    own_half = lax.dynamic_slice_in_dim(half_cycle, aux_index * row_count, row_count, 0)
    sent_half = lax.dynamic_slice_in_dim(half_cycle, (1 - aux_index) * row_count, row_count, 0)
    local_cycle = own_half + lax.ppermute(sent_half, "aux", perm=swap)
    cycle_vals = (cycle_scale * local_cycle).astype(jnp.bfloat16)
    returned = cycle_vals
    ring_offset = jnp.zeros_like(pair_dest)
    ring_scale = 1
    for size, stride in RING_ORDER:
        returned = ring_gather(returned, size, stride, axis_pairs)
        own_coord = (own_index // stride) % size
        dest_coord = (pair_dest // stride) % size
        ring_offset = ring_offset + ((own_coord - dest_coord) % size) * ring_scale
        ring_scale = ring_scale * size
    returned = returned.reshape(axis_pairs, row_count, vir_width)
    own_cycle = jnp.take(returned, ring_offset, axis=0)
    cycle_term = jnp.einsum("pca,pba->pcb", own_cycle, margin, preferred_element_type=jnp.float32)
    updated = prior - cycle_term * inverse
    return updated.astype(jnp.bfloat16)


def solution(mesh):
    placed = (
        P("pair", "aux", None),
        P("pair", "aux", None),
        P("pair", None, None),
        P("pair"),
        P("pair", "aux", None),
        P("pair", None),
        P(),
        P("pair", None),
    )
    return jax.shard_map(
        local, mesh=mesh, in_specs=placed, out_specs=P("pair", "aux", None), check_vma=False
    )
```
